512 devices in a mesh: dp: 16 (over z_hi, x), seq: 32 (over y, z_lo, core).
Axes of the slice: x: 4, y: 4, z: 16 (z_hi: 4, z_lo: 4; z = z_hi * 4 + z_lo), core: 2. Of those that a mesh axis runs over, the one named last changes fastest.
Arguments:
- binned_signals: bfloat16 [16, 16384, 768], P('dp', 'seq'), may hold values from -6 to 6
- kernel_coefficients: bfloat16 [5, 768, 768], P(None, 'dp'), may hold values from -0.09375 to 0.09375
- asking_projector: bfloat16 [768, 256], replicated, may hold values from -0.21875 to 0.21875
- lookup_projector: bfloat16 [768, 256], replicated, may hold values from -0.21875 to 0.21875
- content_projector: bfloat16 [768, 384], replicated, may hold values from -0.21875 to 0.21875
- readout_projector: bfloat16 [384, 768], replicated, may hold values from -0.3125 to 0.3125
- logit_multipliers: float32 [4], replicated, may hold values from 8 to 24
- loss_sensitivity: bfloat16 [16, 4096, 768], P('dp', 'seq'), may hold values from -0.0234375 to 0.0234375
Outputs:
- pooled: bfloat16 [16, 4096, 768], P('dp', 'seq')
- update: float32 [16, 4096, 768], P('dp', 'seq')
- query_grad: float32 [768, 256], replicated
- out_grad: float32 [384, 768], replicated
The draws below stay inside these ranges and needn't reach their ends.
All inputs are finite; a program needn't handle non-finite values.
Results may differ from the reference program's by a relative error of at most 0.0095.
The reference program's roundings to bfloat16 on the way count: a program that leaves them out, or rounds other values in their place, can miss the bound.
Values may be sent and summed in bfloat16 or wider, within the bound.
No kernel may reach another device: no remote copies, remote signals or barrier semaphores. Data moves between devices by JAX's collectives and lax.ppermute only.
A program may use at most 128 MiB of HBM per device.

```python
import math
import jax
import jax.numpy as jnp
from jax import lax

C = 768
TAPS = 5
POOL = 4
LEARNED_ATTENDS = 4
ATTN_PROBE_SPAN = 64
VALUE_SIZE = 96
TOKENS = 4096
BATCH = 16


def block_levels(key, extent, shards, low, top_value):
    loudness = 1.0
    for position, blocks in shards:
        draws = jax.random.uniform(jax.random.fold_in(jax.random.fold_in(key, 6), position), (blocks,), jnp.float32, low / len(shards), top_value / len(shards))
        loudness = loudness * jnp.repeat(jnp.exp(draws), extent[position] // blocks).reshape((-1,) + (1,) * (len(extent) - 1 - position))
    return loudness


def bell_draw(rng, extent, deviation, bound, split=(), kind=jnp.bfloat16):
    drawn = jax.random.normal(rng, extent, jnp.float32) * deviation
    if len(split) > 0:
        drawn = block_levels(rng, extent, split, -0.22, 0.18) * drawn
    return jnp.clip(drawn, min=-bound, max=bound).astype(kind)


def setup_inputs(seed: int = 0) -> dict:
    splits = jax.random.split(jax.random.key(seed), 9)
    binned_signals = bell_draw(splits[0], (BATCH, POOL * TOKENS, C), 1.0, 6.0, ((0, 16), (1, 32)))
    kernel_coefficients = bell_draw(splits[1], (TAPS, C, C), (TAPS * C) ** -0.5, 0.09375, ((1, 16),))
    asking_projector = bell_draw(splits[2], (C, LEARNED_ATTENDS * ATTN_PROBE_SPAN), C ** -0.5, 0.21875)
    lookup_projector = bell_draw(splits[3], (C, LEARNED_ATTENDS * ATTN_PROBE_SPAN), C ** -0.5, 0.21875)
    content_projector = bell_draw(splits[4], (C, LEARNED_ATTENDS * VALUE_SIZE), C ** -0.5, 0.21875)
    readout_projector = bell_draw(splits[5], (LEARNED_ATTENDS * VALUE_SIZE, C), (LEARNED_ATTENDS * VALUE_SIZE) ** -0.5, 0.3125)
    logit_multipliers = jnp.clip(jnp.exp(jax.random.uniform(splits[6], (LEARNED_ATTENDS,), jnp.float32, math.log(8.0), math.log(24.0))), 8.0, 24.0)
    loss_sensitivity = bell_draw(splits[7], (BATCH, TOKENS, C), (BATCH * TOKENS) ** -0.5, 0.0234375, ((0, 16), (1, 32)))
    return dict(binned_signals=binned_signals, kernel_coefficients=kernel_coefficients, asking_projector=asking_projector, lookup_projector=lookup_projector, content_projector=content_projector, readout_projector=readout_projector, logit_multipliers=logit_multipliers, loss_sensitivity=loss_sensitivity)


norm_eps = 1e-05
head_eps = 1e-06

def layer_norm(values):
    centre = lax.optimization_barrier(jnp.mean(values, axis=-1, keepdims=True))
    shifted = values - centre
    variance = lax.optimization_barrier(jnp.mean(shifted * shifted, axis=-1, keepdims=True))
    return shifted * lax.rsqrt(variance + norm_eps)

def activate(values):
    return values * jax.nn.sigmoid(1.702 * values)

def head_norm(values, group_width):
    grouped = values.reshape(values.shape[0], -1, group_width)
    factor = lax.rsqrt(lax.optimization_barrier(jnp.mean(grouped * grouped, axis=-1, keepdims=True)) + head_eps)
    return ((grouped * factor).reshape(values.shape), jnp.broadcast_to(factor, grouped.shape).reshape(values.shape))

def contract_first(former, latter):
    return lax.dot_general(former, latter, (((0,), (0,)), ((), ())), preferred_element_type=jnp.float32)

def contract_last(former, latter):
    return lax.dot_general(former, latter, (((1,), (1,)), ((), ())), preferred_element_type=jnp.float32)

def lone_genome_strand(incoming_tensor, kernel_coefficients, asking_projector, lookup_projector, content_projector, readout_projector, logit_multipliers, directional_perturbations):
    length_fine = incoming_tensor.shape[0]
    channels = incoming_tensor.shape[1]
    margin = TAPS // 2
    activated = activate(layer_norm(incoming_tensor.astype(jnp.float32))).astype(jnp.bfloat16)
    padded = jnp.pad(activated, ((margin, margin), (0, 0)))
    conv_sum = jnp.zeros((length_fine, channels), jnp.float32)
    for tap_index in range(TAPS):
        conv_sum = conv_sum + jnp.dot(padded[tap_index:tap_index + length_fine], kernel_coefficients[tap_index], preferred_element_type=jnp.float32)
    summed = incoming_tensor.astype(jnp.float32) + conv_sum
    pooled = lax.optimization_barrier(jnp.max(summed.reshape(length_fine // POOL, POOL, channels), axis=1)).astype(jnp.bfloat16)
    normed = layer_norm(pooled.astype(jnp.float32)).astype(jnp.bfloat16)
    queries = jnp.dot(normed, asking_projector, preferred_element_type=jnp.float32)
    query_hat, query_factor = head_norm(queries, ATTN_PROBE_SPAN)
    query_unit = query_hat.astype(jnp.bfloat16)
    key_unit = head_norm(jnp.dot(normed, lookup_projector, preferred_element_type=jnp.float32), ATTN_PROBE_SPAN)[0].astype(jnp.bfloat16)
    values_all = jnp.dot(normed, content_projector, preferred_element_type=jnp.float32).astype(jnp.bfloat16)
    heads_grad = contract_last(directional_perturbations, readout_projector).astype(jnp.bfloat16)
    outputs = []
    diffs = []
    for attender_slot in range(LEARNED_ATTENDS):
        key_lo = attender_slot * ATTN_PROBE_SPAN
        value_lo = attender_slot * VALUE_SIZE
        query_part = query_unit[:, key_lo:key_lo + ATTN_PROBE_SPAN]
        key_part = key_unit[:, key_lo:key_lo + ATTN_PROBE_SPAN]
        value_part = values_all[:, value_lo:value_lo + VALUE_SIZE]
        attender_logit_gain = logit_multipliers[attender_slot] / ATTN_PROBE_SPAN
        scores = contract_last(query_part, key_part) * attender_logit_gain
        expo = jnp.exp(scores)
        probs = expo / lax.optimization_barrier(jnp.sum(expo, axis=1, keepdims=True))
        head_out = jnp.dot(probs.astype(jnp.bfloat16), value_part, preferred_element_type=jnp.float32)
        outputs.append(head_out)
        grad_part = heads_grad[:, value_lo:value_lo + VALUE_SIZE]
        prob_grad = contract_last(grad_part, value_part)
        delta = lax.optimization_barrier(jnp.sum(grad_part.astype(jnp.float32) * head_out, axis=1, keepdims=True))
        score_grad = (probs * (prob_grad - delta)).astype(jnp.bfloat16)
        unit_grad = jnp.dot(score_grad, key_part, preferred_element_type=jnp.float32) * attender_logit_gain
        hat_part = query_hat[:, key_lo:key_lo + ATTN_PROBE_SPAN]
        factor_part = query_factor[:, key_lo:key_lo + ATTN_PROBE_SPAN]
        diffs.append(factor_part * (unit_grad - hat_part * lax.optimization_barrier(jnp.mean(hat_part * unit_grad, axis=1, keepdims=True))))
    heads_low = jnp.concatenate(outputs, axis=1).astype(jnp.bfloat16)
    update = jnp.dot(heads_low, readout_projector, preferred_element_type=jnp.float32)
    query_diff = jnp.concatenate(diffs, axis=1).astype(jnp.bfloat16)
    return (pooled, update, contract_first(normed, query_diff), contract_first(heads_low, directional_perturbations))

def reference(binned_signals, kernel_coefficients, asking_projector, lookup_projector, content_projector, readout_projector, logit_multipliers, loss_sensitivity):

    def per_item(coupled_entries):
        return lone_genome_strand(coupled_entries[0], kernel_coefficients, asking_projector, lookup_projector, content_projector, readout_projector, logit_multipliers, coupled_entries[1])
    pooled, update, query_parts, out_parts = lax.map(per_item, (binned_signals, loss_sensitivity))
    return (pooled, update, lax.optimization_barrier(jnp.sum(query_parts, axis=0)), lax.optimization_barrier(jnp.sum(out_parts, axis=0)))
```

```python
import jax
import jax.numpy as jnp
from jax import lax
from jax.sharding import PartitionSpec as P

POOL = 4


norm_eps = 1e-05
head_eps = 1e-06


def padded_2(array, sides, width):
    for axis, dim in sides:
        devices, length = (lax.axis_size(axis), array.shape[dim])
        up = [(i, (i + 1) % devices) for i in range(devices - 1)]
        down = [(j, i) for i, j in up]
        last = lax.slice_in_dim(array, length - width, length, axis=dim)
        leading = lax.slice_in_dim(array, 0, width, axis=dim)
        before = lax.ppermute(last, axis, up)
        after = lax.ppermute(leading, axis, down)
        array = jnp.concatenate([before, array, after], axis=dim)
    return array


DIMS = {
    "core": ("seq", 1, 2),
    "zlo": ("seq", 2, 4),
    "y": ("seq", 8, 4),
    "x": ("dp", 1, 4),
    "zhi": ("dp", 4, 4),
}
RS_ORDER = ("core", "x", "y", "zlo", "zhi")


def coord(dim):
    axis, stride, size = DIMS[dim]
    return (lax.axis_index(axis) // stride) % size


def shift(array, dim, step):
    axis, stride, size = DIMS[dim]
    pairs = []
    for index in range(lax.axis_size(axis)):
        here = (index // stride) % size
        source = index + ((here + step) % size - here) * stride
        pairs.append((source, index))
    return lax.ppermute(array, axis, pairs)


def reduce_scatter_dim(chunks, dim):
    size = DIMS[dim][2]
    me = coord(dim)
    total = lax.dynamic_index_in_dim(chunks, me, 0, keepdims=False)
    for step in range(1, size):
        part = lax.dynamic_index_in_dim(chunks, (me - step) % size, 0, keepdims=False)
        total = total + shift(part, dim, step)
    return total


def gather_dim(array, dim, ordered=True):
    size = DIMS[dim][2]
    stacked = jnp.stack([array] + [shift(array, dim, step) for step in range(1, size)])
    if ordered:
        stacked = jnp.roll(stacked, coord(dim), axis=0)
    return stacked


def all_reduce_flat(flat):
    sizes = [DIMS[dim][2] for dim in RS_ORDER]
    chunks = flat.reshape(*sizes, -1)
    for dim in RS_ORDER:
        chunks = reduce_scatter_dim(chunks, dim)
    for dim in reversed(RS_ORDER):
        chunks = gather_dim(chunks, dim)
    return chunks.reshape(-1)


def layer_norm(values):
    centre = jnp.mean(values, axis=-1, keepdims=True)
    shifted = values - centre
    variance = jnp.mean(shifted * shifted, axis=-1, keepdims=True)
    return shifted * lax.rsqrt(variance + norm_eps)


def activate(values):
    return values * jax.nn.sigmoid(1.702 * values)


def head_norm(values, group_width):
    grouped = values.reshape(values.shape[0], -1, group_width)
    factor = lax.rsqrt(jnp.mean(grouped * grouped, axis=-1, keepdims=True) + head_eps)
    return (
        (grouped * factor).reshape(values.shape),
        jnp.broadcast_to(factor, grouped.shape).reshape(values.shape),
    )


def contract_first(former, latter):
    return lax.dot_general(
        former, latter, (((0,), (0,)), ((), ())), preferred_element_type=jnp.float32
    )


def contract_last(former, latter):
    return lax.dot_general(
        former, latter, (((1,), (1,)), ((), ())), preferred_element_type=jnp.float32
    )


def stacked_conv(padded, all_taps, length_fine):
    tap_count = all_taps.shape[0]
    windows = jnp.concatenate(
        [padded[tap_index : tap_index + length_fine] for tap_index in range(tap_count)], axis=1
    )
    flat_taps = all_taps.reshape(tap_count * all_taps.shape[1], all_taps.shape[2])
    return jnp.dot(windows, flat_taps, preferred_element_type=jnp.float32)


def on_device(
    binned_signals,
    kernel_coefficients,
    asking_projector,
    lookup_projector,
    content_projector,
    readout_projector,
    logit_multipliers,
    loss_sensitivity,
):
    incoming_tensor = binned_signals[0]
    directional_perturbations = loss_sensitivity[0]
    length_fine = incoming_tensor.shape[0]
    channels = incoming_tensor.shape[1]
    tap_count = kernel_coefficients.shape[0]
    margin = tap_count // 2
    attender_total = logit_multipliers.shape[0]
    probe_extent = asking_projector.shape[1] // attender_total
    value_width = content_projector.shape[1] // attender_total
    activated = activate(layer_norm(incoming_tensor.astype(jnp.float32))).astype(jnp.bfloat16)
    padded = padded_2(activated, (("seq", 0),), margin)
    core = coord("core")
    half_width = kernel_coefficients.shape[2] // 2
    own_half = lax.dynamic_slice_in_dim(kernel_coefficients, core * half_width, half_width, axis=2)
    own_taps = lax.all_gather(own_half, "dp", axis=1, tiled=True)
    other_taps = shift(own_taps, "core", 1)
    conv_own = stacked_conv(padded, own_taps, length_fine)
    conv_other = stacked_conv(padded, other_taps, length_fine)
    conv_sum = jnp.where(
        core == 0,
        jnp.concatenate([conv_own, conv_other], axis=1),
        jnp.concatenate([conv_other, conv_own], axis=1),
    )
    summed = incoming_tensor.astype(jnp.float32) + conv_sum
    pooled = jnp.max(summed.reshape(length_fine // POOL, POOL, channels), axis=1).astype(
        jnp.bfloat16
    )
    normed = layer_norm(pooled.astype(jnp.float32)).astype(jnp.bfloat16)
    queries = jnp.dot(normed, asking_projector, preferred_element_type=jnp.float32)
    query_hat, query_factor = head_norm(queries, probe_extent)
    query_unit = query_hat.astype(jnp.bfloat16)
    key_local = head_norm(
        jnp.dot(normed, lookup_projector, preferred_element_type=jnp.float32), probe_extent
    )[0].astype(jnp.bfloat16)
    value_local = jnp.dot(normed, content_projector, preferred_element_type=jnp.float32).astype(
        jnp.bfloat16
    )
    key_width = key_local.shape[1]
    joined = jnp.concatenate([key_local, value_local], axis=1)
    for dim in ("zlo", "y", "core"):
        joined = gather_dim(joined, dim, ordered=False)
    joined = joined.reshape(-1, joined.shape[-1])
    key_unit, values_all = joined[:, :key_width], joined[:, key_width:]
    heads_grad = contract_last(directional_perturbations, readout_projector).astype(jnp.bfloat16)
    outputs = []
    diffs = []
    for attender_slot in range(attender_total):
        key_lo = attender_slot * probe_extent
        value_lo = attender_slot * value_width
        query_part = query_unit[:, key_lo : key_lo + probe_extent]
        key_part = key_unit[:, key_lo : key_lo + probe_extent]
        value_part = values_all[:, value_lo : value_lo + value_width]
        attender_logit_gain = logit_multipliers[attender_slot] / probe_extent
        scores = contract_last(query_part, key_part) * attender_logit_gain
        expo = jnp.exp(scores)
        probs = expo / jnp.sum(expo, axis=1, keepdims=True)
        head_out = jnp.dot(
            probs.astype(jnp.bfloat16), value_part, preferred_element_type=jnp.float32
        )
        outputs.append(head_out)
        grad_part = heads_grad[:, value_lo : value_lo + value_width]
        prob_grad = contract_last(grad_part, value_part)
        delta = jnp.sum(grad_part.astype(jnp.float32) * head_out, axis=1, keepdims=True)
        score_grad = (probs * (prob_grad - delta)).astype(jnp.bfloat16)
        unit_grad = (
            jnp.dot(score_grad, key_part, preferred_element_type=jnp.float32) * attender_logit_gain
        )
        hat_part = query_hat[:, key_lo : key_lo + probe_extent]
        factor_part = query_factor[:, key_lo : key_lo + probe_extent]
        diffs.append(
            factor_part
            * (unit_grad - hat_part * jnp.mean(hat_part * unit_grad, axis=1, keepdims=True))
        )
    heads_low = jnp.concatenate(outputs, axis=1).astype(jnp.bfloat16)
    update = jnp.dot(heads_low, readout_projector, preferred_element_type=jnp.float32)
    query_diff = jnp.concatenate(diffs, axis=1).astype(jnp.bfloat16)
    query_local = contract_first(normed, query_diff)
    out_local = contract_first(heads_low, directional_perturbations)
    flat = all_reduce_flat(jnp.concatenate([query_local.reshape(-1), out_local.reshape(-1)]))
    query_grad = flat[: query_local.size].reshape(query_local.shape)
    out_grad = flat[query_local.size :].reshape(out_local.shape)
    return (pooled[None], update[None], query_grad, out_grad)


def solution(mesh):
    return jax.shard_map(
        on_device,
        mesh=mesh,
        in_specs=(
            P("dp", "seq", None),
            P(None, "dp", None),
            P(),
            P(),
            P(),
            P(),
            P(),
            P("dp", "seq", None),
        ),
        out_specs=(P("dp", "seq", None), P("dp", "seq", None), P(), P()),
        check_vma=False,
    )
```

```python
import jax
import jax.numpy as jnp
from jax import lax
from jax.sharding import PartitionSpec as P

POOL = 4


norm_eps = 1e-05
head_eps = 1e-06


def padded_2(array, sides, width):
    for axis, dim in sides:
        devices, length = (lax.axis_size(axis), array.shape[dim])
        up = [(i, (i + 1) % devices) for i in range(devices - 1)]
        down = [(j, i) for i, j in up]
        last = lax.slice_in_dim(array, length - width, length, axis=dim)
        leading = lax.slice_in_dim(array, 0, width, axis=dim)
        before = lax.ppermute(last, axis, up)
        after = lax.ppermute(leading, axis, down)
        array = jnp.concatenate([before, array, after], axis=dim)
    return array


DIMS = {
    "core": ("seq", 1, 2),
    "zlo": ("seq", 2, 4),
    "y": ("seq", 8, 4),
    "x": ("dp", 1, 4),
    "zhi": ("dp", 4, 4),
}
RS_ORDER = ("core", "x", "y")
SUM_ORDER = ("zlo", "zhi")


def coord(dim):
    axis, stride, size = DIMS[dim]
    return (lax.axis_index(axis) // stride) % size


def shift(array, dim, step):
    axis, stride, size = DIMS[dim]
    pairs = []
    for index in range(lax.axis_size(axis)):
        here = (index // stride) % size
        source = index + ((here + step) % size - here) * stride
        pairs.append((source, index))
    return lax.ppermute(array, axis, pairs)


def reduce_scatter_dim(chunks, dim):
    size = DIMS[dim][2]
    me = coord(dim)
    total = lax.dynamic_index_in_dim(chunks, me, 0, keepdims=False)
    for step in range(1, size):
        part = lax.dynamic_index_in_dim(chunks, (me - step) % size, 0, keepdims=False)
        total = total + shift(part, dim, step)
    return total


def gather_dim(array, dim, ordered=True):
    size = DIMS[dim][2]
    stacked = jnp.stack([array] + [shift(array, dim, step) for step in range(1, size)])
    if ordered:
        stacked = jnp.roll(stacked, coord(dim), axis=0)
    return stacked


def swap_y_pair(array):
    axis, stride, _ = DIMS["y"]
    pairs = []
    for index in range(lax.axis_size(axis)):
        here = (index // stride) % 4
        pairs.append((index + ((here ^ 1) - here) * stride, index))
    return lax.ppermute(array, axis, pairs)


def sum_in_order(stacked):
    total = stacked[0]
    for index in range(1, stacked.shape[0]):
        total = total + stacked[index]
    return total


def all_reduce_flat(flat):
    sizes = [DIMS[dim][2] for dim in RS_ORDER]
    chunks = flat.reshape(*sizes, -1)
    for dim in RS_ORDER:
        chunks = reduce_scatter_dim(chunks, dim)
    for dim in SUM_ORDER:
        chunks = sum_in_order(gather_dim(chunks, dim))
    for dim in reversed(RS_ORDER):
        chunks = gather_dim(chunks, dim)
    return chunks.reshape(-1)


def layer_norm(values):
    centre = jnp.mean(values, axis=-1, keepdims=True)
    shifted = values - centre
    variance = jnp.mean(shifted * shifted, axis=-1, keepdims=True)
    return shifted * lax.rsqrt(variance + norm_eps)


def activate(values):
    return values * jax.nn.sigmoid(1.702 * values)


def head_norm(values, group_width):
    grouped = values.reshape(values.shape[0], -1, group_width)
    factor = lax.rsqrt(jnp.mean(grouped * grouped, axis=-1, keepdims=True) + head_eps)
    return (
        (grouped * factor).reshape(values.shape),
        jnp.broadcast_to(factor, grouped.shape).reshape(values.shape),
    )


def contract_first(former, latter):
    return lax.dot_general(
        former, latter, (((0,), (0,)), ((), ())), preferred_element_type=jnp.float32
    )


def contract_last(former, latter):
    return lax.dot_general(
        former, latter, (((1,), (1,)), ((), ())), preferred_element_type=jnp.float32
    )


def stacked_conv(padded, all_taps, length_fine):
    tap_count = all_taps.shape[0]
    windows = jnp.concatenate(
        [padded[tap_index : tap_index + length_fine] for tap_index in range(tap_count)], axis=1
    )
    flat_taps = all_taps.reshape(tap_count * all_taps.shape[1], all_taps.shape[2])
    return jnp.dot(windows, flat_taps, preferred_element_type=jnp.float32)


def on_device(
    binned_signals,
    kernel_coefficients,
    asking_projector,
    lookup_projector,
    content_projector,
    readout_projector,
    logit_multipliers,
    loss_sensitivity,
):
    incoming_tensor = binned_signals[0]
    directional_perturbations = loss_sensitivity[0]
    length_fine = incoming_tensor.shape[0]
    channels = incoming_tensor.shape[1]
    tap_count = kernel_coefficients.shape[0]
    margin = tap_count // 2
    attender_total = logit_multipliers.shape[0]
    probe_extent = asking_projector.shape[1] // attender_total
    value_width = content_projector.shape[1] // attender_total
    activated = activate(layer_norm(incoming_tensor.astype(jnp.float32))).astype(jnp.bfloat16)
    padded = padded_2(activated, (("seq", 0),), margin)
    core = coord("core")
    low_bit = coord("y") % 2
    quarter = kernel_coefficients.shape[2] // 4
    own_part = lax.dynamic_slice_in_dim(
        kernel_coefficients, (2 * core + low_bit) * quarter, quarter, axis=2
    )
    own_taps = lax.all_gather(own_part, "dp", axis=1, tiled=True)
    pair_taps = swap_y_pair(own_taps)
    near_taps = jnp.concatenate([own_taps, pair_taps], axis=2)
    far_taps = jnp.concatenate(
        [shift(own_taps, "core", 1), shift(pair_taps, "core", 1)], axis=2
    )
    conv_near = stacked_conv(padded, near_taps, length_fine)
    conv_far = stacked_conv(padded, far_taps, length_fine)

    def in_order(pieces_conv):
        first, second = pieces_conv[:, :quarter], pieces_conv[:, quarter:]
        return jnp.where(
            low_bit == 0,
            jnp.concatenate([first, second], axis=1),
            jnp.concatenate([second, first], axis=1),
        )

    conv_near, conv_far = in_order(conv_near), in_order(conv_far)
    conv_sum = jnp.where(
        core == 0,
        jnp.concatenate([conv_near, conv_far], axis=1),
        jnp.concatenate([conv_far, conv_near], axis=1),
    )
    summed = incoming_tensor.astype(jnp.float32) + conv_sum
    pooled = jnp.max(summed.reshape(length_fine // POOL, POOL, channels), axis=1).astype(
        jnp.bfloat16
    )
    normed = layer_norm(pooled.astype(jnp.float32)).astype(jnp.bfloat16)
    queries = jnp.dot(normed, asking_projector, preferred_element_type=jnp.float32)
    query_hat, query_factor = head_norm(queries, probe_extent)
    query_unit = query_hat.astype(jnp.bfloat16)
    key_local = head_norm(
        jnp.dot(normed, lookup_projector, preferred_element_type=jnp.float32), probe_extent
    )[0].astype(jnp.bfloat16)
    value_local = jnp.dot(normed, content_projector, preferred_element_type=jnp.float32).astype(
        jnp.bfloat16
    )
    key_width = key_local.shape[1]
    joined = jnp.concatenate([key_local, value_local], axis=1)
    for dim in ("zlo", "y", "core"):
        joined = gather_dim(joined, dim, ordered=False)
    joined = joined.reshape(-1, joined.shape[-1])
    key_unit, values_all = joined[:, :key_width], joined[:, key_width:]
    heads_grad = contract_last(directional_perturbations, readout_projector).astype(jnp.bfloat16)
    outputs = []
    diffs = []
    for attender_slot in range(attender_total):
        key_lo = attender_slot * probe_extent
        value_lo = attender_slot * value_width
        query_part = query_unit[:, key_lo : key_lo + probe_extent]
        key_part = key_unit[:, key_lo : key_lo + probe_extent]
        value_part = values_all[:, value_lo : value_lo + value_width]
        attender_logit_gain = logit_multipliers[attender_slot] / probe_extent
        scores = contract_last(query_part, key_part) * attender_logit_gain
        expo = jnp.exp(scores)
        probs = expo / jnp.sum(expo, axis=1, keepdims=True)
        head_out = jnp.dot(
            probs.astype(jnp.bfloat16), value_part, preferred_element_type=jnp.float32
        )
        outputs.append(head_out)
        grad_part = heads_grad[:, value_lo : value_lo + value_width]
        prob_grad = contract_last(grad_part, value_part)
        delta = jnp.sum(grad_part.astype(jnp.float32) * head_out, axis=1, keepdims=True)
        score_grad = (probs * (prob_grad - delta)).astype(jnp.bfloat16)
        unit_grad = (
            jnp.dot(score_grad, key_part, preferred_element_type=jnp.float32) * attender_logit_gain
        )
        hat_part = query_hat[:, key_lo : key_lo + probe_extent]
        factor_part = query_factor[:, key_lo : key_lo + probe_extent]
        diffs.append(
            factor_part
            * (unit_grad - hat_part * jnp.mean(hat_part * unit_grad, axis=1, keepdims=True))
        )
    heads_low = jnp.concatenate(outputs, axis=1).astype(jnp.bfloat16)
    update = jnp.dot(heads_low, readout_projector, preferred_element_type=jnp.float32)
    query_diff = jnp.concatenate(diffs, axis=1).astype(jnp.bfloat16)
    query_local = contract_first(normed, query_diff)
    out_local = contract_first(heads_low, directional_perturbations)
    flat = all_reduce_flat(jnp.concatenate([query_local.reshape(-1), out_local.reshape(-1)]))
    query_grad = flat[: query_local.size].reshape(query_local.shape)
    out_grad = flat[query_local.size :].reshape(out_local.shape)
    return (pooled[None], update[None], query_grad, out_grad)


def solution(mesh):
    return jax.shard_map(
        on_device,
        mesh=mesh,
        in_specs=(
            P("dp", "seq", None),
            P(None, "dp", None),
            P(),
            P(),
            P(),
            P(),
            P(),
            P("dp", "seq", None),
        ),
        out_specs=(P("dp", "seq", None), P("dp", "seq", None), P(), P()),
        check_vma=False,
    )
```

```python
import jax
import jax.numpy as jnp
from jax import lax
from jax.sharding import PartitionSpec as P

POOL = 4


norm_eps = 1e-05
head_eps = 1e-06


def padded_2(array, sides, width):
    for axis, dim in sides:
        devices, length = (lax.axis_size(axis), array.shape[dim])
        up = [(i, (i + 1) % devices) for i in range(devices - 1)]
        down = [(j, i) for i, j in up]
        last = lax.slice_in_dim(array, length - width, length, axis=dim)
        leading = lax.slice_in_dim(array, 0, width, axis=dim)
        before = lax.ppermute(last, axis, up)
        after = lax.ppermute(leading, axis, down)
        array = jnp.concatenate([before, array, after], axis=dim)
    return array


DIMS = {
    "core": ("seq", 1, 2),
    "zlo": ("seq", 2, 4),
    "y": ("seq", 8, 4),
    "x": ("dp", 1, 4),
    "zhi": ("dp", 4, 4),
}
RS_ORDER = ("core", "x", "y")
SUM_ORDER = ("zlo", "zhi")


def coord(dim):
    axis, stride, size = DIMS[dim]
    return (lax.axis_index(axis) // stride) % size


def shift(array, dim, step):
    axis, stride, size = DIMS[dim]
    pairs = []
    for index in range(lax.axis_size(axis)):
        here = (index // stride) % size
        source = index + ((here + step) % size - here) * stride
        pairs.append((source, index))
    return lax.ppermute(array, axis, pairs)


def reduce_scatter_dim(chunks, dim):
    size = DIMS[dim][2]
    me = coord(dim)
    total = lax.dynamic_index_in_dim(chunks, me, 0, keepdims=False)
    for step in range(1, size):
        part = lax.dynamic_index_in_dim(chunks, (me - step) % size, 0, keepdims=False)
        total = total + shift(part, dim, step)
    return total


def gather_dim(array, dim, ordered=True):
    size = DIMS[dim][2]
    stacked = jnp.stack([array] + [shift(array, dim, step) for step in range(1, size)])
    if ordered:
        slots = (jnp.arange(size) - coord(dim)) % size
        stacked = jnp.take(stacked, slots, axis=0)
    return stacked


def sum_in_order(stacked):
    total = stacked[0]
    for index in range(1, stacked.shape[0]):
        total = total + stacked[index]
    return total


def all_reduce_flat(flat):
    sizes = [DIMS[dim][2] for dim in RS_ORDER]
    chunks = flat.reshape(*sizes, -1)
    for dim in RS_ORDER:
        chunks = reduce_scatter_dim(chunks, dim)
    for dim in SUM_ORDER:
        chunks = sum_in_order(gather_dim(chunks, dim))
    for dim in reversed(RS_ORDER):
        chunks = gather_dim(chunks, dim)
    return chunks.reshape(-1)


def layer_norm(values):
    centre = jnp.mean(values, axis=-1, keepdims=True)
    shifted = values - centre
    variance = jnp.mean(shifted * shifted, axis=-1, keepdims=True)
    return shifted * lax.rsqrt(variance + norm_eps)


def activate(values):
    return values * jax.nn.sigmoid(1.702 * values)


def head_norm(values, group_width):
    grouped = values.reshape(values.shape[0], -1, group_width)
    factor = lax.rsqrt(jnp.mean(grouped * grouped, axis=-1, keepdims=True) + head_eps)
    return (
        (grouped * factor).reshape(values.shape),
        jnp.broadcast_to(factor, grouped.shape).reshape(values.shape),
    )


def contract_first(former, latter):
    return lax.dot_general(
        former, latter, (((0,), (0,)), ((), ())), preferred_element_type=jnp.float32
    )


def contract_last(former, latter):
    return lax.dot_general(
        former, latter, (((1,), (1,)), ((), ())), preferred_element_type=jnp.float32
    )


def stacked_conv(padded, all_taps, length_fine):
    tap_count = all_taps.shape[0]
    windows = jnp.concatenate(
        [padded[tap_index : tap_index + length_fine] for tap_index in range(tap_count)], axis=1
    )
    flat_taps = all_taps.reshape(tap_count * all_taps.shape[1], all_taps.shape[2])
    return jnp.dot(windows, flat_taps, preferred_element_type=jnp.float32)


def on_device(
    binned_signals,
    kernel_coefficients,
    asking_projector,
    lookup_projector,
    content_projector,
    readout_projector,
    logit_multipliers,
    loss_sensitivity,
):
    incoming_tensor = binned_signals[0]
    directional_perturbations = loss_sensitivity[0]
    length_fine = incoming_tensor.shape[0]
    channels = incoming_tensor.shape[1]
    tap_count = kernel_coefficients.shape[0]
    margin = tap_count // 2
    attender_total = logit_multipliers.shape[0]
    probe_extent = asking_projector.shape[1] // attender_total
    value_width = content_projector.shape[1] // attender_total
    activated = activate(layer_norm(incoming_tensor.astype(jnp.float32))).astype(jnp.bfloat16)
    padded = padded_2(activated, (("seq", 0),), margin)
    core = coord("core")
    half_width = kernel_coefficients.shape[2] // 2
    own_half = lax.dynamic_slice_in_dim(kernel_coefficients, core * half_width, half_width, axis=2)
    own_taps = lax.all_gather(own_half, "dp", axis=1, tiled=True)
    other_taps = shift(own_taps, "core", 1)
    conv_own = stacked_conv(padded, own_taps, length_fine)
    conv_other = stacked_conv(padded, other_taps, length_fine)
    conv_sum = jnp.where(
        core == 0,
        jnp.concatenate([conv_own, conv_other], axis=1),
        jnp.concatenate([conv_other, conv_own], axis=1),
    )
    summed = incoming_tensor.astype(jnp.float32) + conv_sum
    pooled = jnp.max(summed.reshape(length_fine // POOL, POOL, channels), axis=1).astype(
        jnp.bfloat16
    )
    normed = layer_norm(pooled.astype(jnp.float32)).astype(jnp.bfloat16)
    queries = jnp.dot(normed, asking_projector, preferred_element_type=jnp.float32)
    query_hat, query_factor = head_norm(queries, probe_extent)
    query_unit = query_hat.astype(jnp.bfloat16)
    key_local = head_norm(
        jnp.dot(normed, lookup_projector, preferred_element_type=jnp.float32), probe_extent
    )[0].astype(jnp.bfloat16)
    value_local = jnp.dot(normed, content_projector, preferred_element_type=jnp.float32).astype(
        jnp.bfloat16
    )
    key_width = key_local.shape[1]
    joined = jnp.concatenate([key_local, value_local], axis=1)
    for dim in ("zlo", "y", "core"):
        joined = gather_dim(joined, dim, ordered=False)
    joined = joined.reshape(-1, joined.shape[-1])
    key_unit, values_all = joined[:, :key_width], joined[:, key_width:]
    heads_grad = contract_last(directional_perturbations, readout_projector).astype(jnp.bfloat16)
    outputs = []
    diffs = []
    for attender_slot in range(attender_total):
        key_lo = attender_slot * probe_extent
        value_lo = attender_slot * value_width
        query_part = query_unit[:, key_lo : key_lo + probe_extent]
        key_part = key_unit[:, key_lo : key_lo + probe_extent]
        value_part = values_all[:, value_lo : value_lo + value_width]
        attender_logit_gain = logit_multipliers[attender_slot] / probe_extent
        scores = contract_last(query_part, key_part) * attender_logit_gain
        expo = jnp.exp(scores)
        probs = expo / jnp.sum(expo, axis=1, keepdims=True)
        head_out = jnp.dot(
            probs.astype(jnp.bfloat16), value_part, preferred_element_type=jnp.float32
        )
        outputs.append(head_out)
        grad_part = heads_grad[:, value_lo : value_lo + value_width]
        prob_grad = contract_last(grad_part, value_part)
        delta = jnp.sum(grad_part.astype(jnp.float32) * head_out, axis=1, keepdims=True)
        score_grad = (probs * (prob_grad - delta)).astype(jnp.bfloat16)
        unit_grad = (
            jnp.dot(score_grad, key_part, preferred_element_type=jnp.float32) * attender_logit_gain
        )
        hat_part = query_hat[:, key_lo : key_lo + probe_extent]
        factor_part = query_factor[:, key_lo : key_lo + probe_extent]
        diffs.append(
            factor_part
            * (unit_grad - hat_part * jnp.mean(hat_part * unit_grad, axis=1, keepdims=True))
        )
    heads_low = jnp.concatenate(outputs, axis=1).astype(jnp.bfloat16)
    update = jnp.dot(heads_low, readout_projector, preferred_element_type=jnp.float32)
    query_diff = jnp.concatenate(diffs, axis=1).astype(jnp.bfloat16)
    query_local = contract_first(normed, query_diff)
    out_local = contract_first(heads_low, directional_perturbations)
    flat = all_reduce_flat(jnp.concatenate([query_local.reshape(-1), out_local.reshape(-1)]))
    query_grad = flat[: query_local.size].reshape(query_local.shape)
    out_grad = flat[query_local.size :].reshape(out_local.shape)
    return (pooled[None], update[None], query_grad, out_grad)


def solution(mesh):
    return jax.shard_map(
        on_device,
        mesh=mesh,
        in_specs=(
            P("dp", "seq", None),
            P(None, "dp", None),
            P(),
            P(),
            P(),
            P(),
            P(),
            P("dp", "seq", None),
        ),
        out_specs=(P("dp", "seq", None), P("dp", "seq", None), P(), P()),
        check_vma=False,
    )
```

```python
import jax
import jax.numpy as jnp
from jax import lax
from jax.sharding import PartitionSpec as P

POOL = 4


norm_eps = 1e-05
head_eps = 1e-06


def padded_2(array, sides, width):
    for axis, dim in sides:
        devices, length = (lax.axis_size(axis), array.shape[dim])
        up = [(i, (i + 1) % devices) for i in range(devices - 1)]
        down = [(j, i) for i, j in up]
        last = lax.slice_in_dim(array, length - width, length, axis=dim)
        leading = lax.slice_in_dim(array, 0, width, axis=dim)
        before = lax.ppermute(last, axis, up)
        after = lax.ppermute(leading, axis, down)
        array = jnp.concatenate([before, array, after], axis=dim)
    return array


DIMS = {
    "core": ("seq", 1, 2),
    "zlo": ("seq", 2, 4),
    "y": ("seq", 8, 4),
    "x": ("dp", 1, 4),
    "zhi": ("dp", 4, 4),
}
RS_ORDER = ("core", "x", "y")
SUM_ORDER = ("zlo", "zhi")


def coord(dim):
    axis, stride, size = DIMS[dim]
    return (lax.axis_index(axis) // stride) % size


def shift(array, dim, step):
    axis, stride, size = DIMS[dim]
    pairs = []
    for index in range(lax.axis_size(axis)):
        here = (index // stride) % size
        source = index + ((here + step) % size - here) * stride
        pairs.append((source, index))
    return lax.ppermute(array, axis, pairs)


def reduce_scatter_dim(chunks, dim):
    size = DIMS[dim][2]
    me = coord(dim)
    total = lax.dynamic_index_in_dim(chunks, me, 0, keepdims=False)
    for step in range(1, size):
        part = lax.dynamic_index_in_dim(chunks, (me - step) % size, 0, keepdims=False)
        total = total + shift(part, dim, step)
    return total


def gather_dim(array, dim, ordered=True):
    size = DIMS[dim][2]
    stacked = jnp.stack([array] + [shift(array, dim, step) for step in range(1, size)])
    if ordered:
        slots = (jnp.arange(size) - coord(dim)) % size
        stacked = jnp.take(stacked, slots, axis=0, mode="clip")
    return stacked


def sum_in_order(stacked):
    total = stacked[0]
    for index in range(1, stacked.shape[0]):
        total = total + stacked[index]
    return total


def all_reduce_flat(flat):
    sizes = [DIMS[dim][2] for dim in RS_ORDER]
    chunks = flat.reshape(*sizes, -1)
    for dim in RS_ORDER:
        chunks = reduce_scatter_dim(chunks, dim)
    for dim in SUM_ORDER:
        chunks = sum_in_order(gather_dim(chunks, dim))
    for dim in reversed(RS_ORDER):
        chunks = gather_dim(chunks, dim)
    return chunks.reshape(-1)


def layer_norm(values):
    centre = jnp.mean(values, axis=-1, keepdims=True)
    shifted = values - centre
    variance = jnp.mean(shifted * shifted, axis=-1, keepdims=True)
    return shifted * lax.rsqrt(variance + norm_eps)


def activate(values):
    return values * jax.nn.sigmoid(1.702 * values)


def head_norm(values, group_width):
    grouped = values.reshape(values.shape[0], -1, group_width)
    factor = lax.rsqrt(jnp.mean(grouped * grouped, axis=-1, keepdims=True) + head_eps)
    return (
        (grouped * factor).reshape(values.shape),
        jnp.broadcast_to(factor, grouped.shape).reshape(values.shape),
    )


def contract_first(former, latter):
    return lax.dot_general(
        former, latter, (((0,), (0,)), ((), ())), preferred_element_type=jnp.float32
    )


def contract_last(former, latter):
    return lax.dot_general(
        former, latter, (((1,), (1,)), ((), ())), preferred_element_type=jnp.float32
    )


def stacked_conv(padded, all_taps, length_fine):
    tap_count = all_taps.shape[0]
    windows = jnp.concatenate(
        [padded[tap_index : tap_index + length_fine] for tap_index in range(tap_count)], axis=1
    )
    flat_taps = all_taps.reshape(tap_count * all_taps.shape[1], all_taps.shape[2])
    return jnp.dot(windows, flat_taps, preferred_element_type=jnp.float32)


def on_device(
    binned_signals,
    kernel_coefficients,
    asking_projector,
    lookup_projector,
    content_projector,
    readout_projector,
    logit_multipliers,
    loss_sensitivity,
):
    incoming_tensor = binned_signals[0]
    directional_perturbations = loss_sensitivity[0]
    length_fine = incoming_tensor.shape[0]
    channels = incoming_tensor.shape[1]
    tap_count = kernel_coefficients.shape[0]
    margin = tap_count // 2
    attender_total = logit_multipliers.shape[0]
    probe_extent = asking_projector.shape[1] // attender_total
    value_width = content_projector.shape[1] // attender_total
    activated = activate(layer_norm(incoming_tensor.astype(jnp.float32))).astype(jnp.bfloat16)
    padded = padded_2(activated, (("seq", 0),), margin)
    core = coord("core")
    quarter = kernel_coefficients.shape[2] // 4
    first_part = lax.dynamic_slice_in_dim(kernel_coefficients, 2 * core * quarter, quarter, axis=2)
    second_part = lax.dynamic_slice_in_dim(
        kernel_coefficients, (2 * core + 1) * quarter, quarter, axis=2
    )
    first_taps = lax.all_gather(first_part, "dp", axis=1, tiled=True)
    routed = gather_dim(gather_dim(second_part, "x"), "zhi")
    blocks = routed.shape[0] * routed.shape[1]
    routed = routed.reshape(blocks, *second_part.shape)
    second_taps = jnp.moveaxis(routed, 0, 1).reshape(first_taps.shape)
    own_taps = jnp.concatenate([first_taps, second_taps], axis=2)
    other_taps = shift(own_taps, "core", 1)
    conv_own = stacked_conv(padded, own_taps, length_fine)
    conv_other = stacked_conv(padded, other_taps, length_fine)
    conv_sum = jnp.where(
        core == 0,
        jnp.concatenate([conv_own, conv_other], axis=1),
        jnp.concatenate([conv_other, conv_own], axis=1),
    )
    summed = incoming_tensor.astype(jnp.float32) + conv_sum
    pooled = jnp.max(summed.reshape(length_fine // POOL, POOL, channels), axis=1).astype(
        jnp.bfloat16
    )
    normed = layer_norm(pooled.astype(jnp.float32)).astype(jnp.bfloat16)
    queries = jnp.dot(normed, asking_projector, preferred_element_type=jnp.float32)
    query_hat, query_factor = head_norm(queries, probe_extent)
    query_unit = query_hat.astype(jnp.bfloat16)
    key_local = head_norm(
        jnp.dot(normed, lookup_projector, preferred_element_type=jnp.float32), probe_extent
    )[0].astype(jnp.bfloat16)
    value_local = jnp.dot(normed, content_projector, preferred_element_type=jnp.float32).astype(
        jnp.bfloat16
    )
    key_width = key_local.shape[1]
    joined = jnp.concatenate([key_local, value_local], axis=1)
    for dim in ("zlo", "y", "core"):
        joined = gather_dim(joined, dim, ordered=False)
    joined = joined.reshape(-1, joined.shape[-1])
    key_unit, values_all = joined[:, :key_width], joined[:, key_width:]
    heads_grad = contract_last(directional_perturbations, readout_projector).astype(jnp.bfloat16)
    outputs = []
    diffs = []
    for attender_slot in range(attender_total):
        key_lo = attender_slot * probe_extent
        value_lo = attender_slot * value_width
        query_part = query_unit[:, key_lo : key_lo + probe_extent]
        key_part = key_unit[:, key_lo : key_lo + probe_extent]
        value_part = values_all[:, value_lo : value_lo + value_width]
        attender_logit_gain = logit_multipliers[attender_slot] / probe_extent
        scores = contract_last(query_part, key_part) * attender_logit_gain
        expo = jnp.exp(scores)
        probs = expo / jnp.sum(expo, axis=1, keepdims=True)
        head_out = jnp.dot(
            probs.astype(jnp.bfloat16), value_part, preferred_element_type=jnp.float32
        )
        outputs.append(head_out)
        grad_part = heads_grad[:, value_lo : value_lo + value_width]
        prob_grad = contract_last(grad_part, value_part)
        delta = jnp.sum(grad_part.astype(jnp.float32) * head_out, axis=1, keepdims=True)
        score_grad = (probs * (prob_grad - delta)).astype(jnp.bfloat16)
        unit_grad = (
            jnp.dot(score_grad, key_part, preferred_element_type=jnp.float32) * attender_logit_gain
        )
        hat_part = query_hat[:, key_lo : key_lo + probe_extent]
        factor_part = query_factor[:, key_lo : key_lo + probe_extent]
        diffs.append(
            factor_part
            * (unit_grad - hat_part * jnp.mean(hat_part * unit_grad, axis=1, keepdims=True))
        )
    heads_low = jnp.concatenate(outputs, axis=1).astype(jnp.bfloat16)
    update = jnp.dot(heads_low, readout_projector, preferred_element_type=jnp.float32)
    query_diff = jnp.concatenate(diffs, axis=1).astype(jnp.bfloat16)
    query_local = contract_first(normed, query_diff)
    out_local = contract_first(heads_low, directional_perturbations)
    flat = all_reduce_flat(jnp.concatenate([query_local.reshape(-1), out_local.reshape(-1)]))
    query_grad = flat[: query_local.size].reshape(query_local.shape)
    out_grad = flat[query_local.size :].reshape(out_local.shape)
    return (pooled[None], update[None], query_grad, out_grad)


def solution(mesh):
    return jax.shard_map(
        on_device,
        mesh=mesh,
        in_specs=(
            P("dp", "seq", None),
            P(None, "dp", None),
            P(),
            P(),
            P(),
            P(),
            P(),
            P("dp", "seq", None),
        ),
        out_specs=(P("dp", "seq", None), P("dp", "seq", None), P(), P()),
        check_vma=False,
    )
```

```python
import jax
import jax.numpy as jnp
from jax import lax
from jax.sharding import PartitionSpec as P

POOL = 4


norm_eps = 1e-05
head_eps = 1e-06


def padded_2(array, sides, width):
    for axis, dim in sides:
        devices, length = (lax.axis_size(axis), array.shape[dim])
        up = [(i, (i + 1) % devices) for i in range(devices - 1)]
        down = [(j, i) for i, j in up]
        last = lax.slice_in_dim(array, length - width, length, axis=dim)
        leading = lax.slice_in_dim(array, 0, width, axis=dim)
        before = lax.ppermute(last, axis, up)
        after = lax.ppermute(leading, axis, down)
        array = jnp.concatenate([before, array, after], axis=dim)
    return array


DIMS = {
    "core": ("seq", 1, 2),
    "zlo": ("seq", 2, 4),
    "y": ("seq", 8, 4),
    "x": ("dp", 1, 4),
    "zhi": ("dp", 4, 4),
}
RS_ORDER = ("core", "x", "y")
SUM_ORDER = ("zlo", "zhi")


def coord(dim):
    axis, stride, size = DIMS[dim]
    return (lax.axis_index(axis) // stride) % size


def shift(array, dim, step):
    axis, stride, size = DIMS[dim]
    pairs = []
    for index in range(lax.axis_size(axis)):
        here = (index // stride) % size
        source = index + ((here + step) % size - here) * stride
        pairs.append((source, index))
    return lax.ppermute(array, axis, pairs)


def reduce_scatter_dim(chunks, dim):
    size = DIMS[dim][2]
    me = coord(dim)
    total = lax.dynamic_index_in_dim(chunks, me, 0, keepdims=False)
    for step in range(1, size):
        part = lax.dynamic_index_in_dim(chunks, (me - step) % size, 0, keepdims=False)
        total = total + shift(part, dim, step)
    return total


def gather_dim(array, dim, ordered=True):
    size = DIMS[dim][2]
    stacked = jnp.stack([array] + [shift(array, dim, step) for step in range(1, size)])
    if ordered:
        slots = (jnp.arange(size) - coord(dim)) % size
        stacked = jnp.take(stacked, slots, axis=0, mode="clip")
    return stacked


def sum_in_order(stacked):
    total = stacked[0]
    for index in range(1, stacked.shape[0]):
        total = total + stacked[index]
    return total


def all_reduce_flat(flat):
    sizes = [DIMS[dim][2] for dim in RS_ORDER]
    chunks = flat.reshape(*sizes, -1)
    for dim in RS_ORDER:
        chunks = reduce_scatter_dim(chunks, dim)
    for dim in SUM_ORDER:
        chunks = sum_in_order(gather_dim(chunks, dim))
    for dim in reversed(RS_ORDER):
        chunks = gather_dim(chunks, dim)
    return chunks.reshape(-1)


def layer_norm(values):
    centre = jnp.mean(values, axis=-1, keepdims=True)
    shifted = values - centre
    variance = jnp.mean(shifted * shifted, axis=-1, keepdims=True)
    return shifted * lax.rsqrt(variance + norm_eps)


def activate(values):
    return values * jax.nn.sigmoid(1.702 * values)


def head_norm(values, group_width):
    grouped = values.reshape(values.shape[0], -1, group_width)
    factor = lax.rsqrt(jnp.mean(grouped * grouped, axis=-1, keepdims=True) + head_eps)
    return (
        (grouped * factor).reshape(values.shape),
        jnp.broadcast_to(factor, grouped.shape).reshape(values.shape),
    )


def contract_first(former, latter):
    return lax.dot_general(
        former, latter, (((0,), (0,)), ((), ())), preferred_element_type=jnp.float32
    )


def contract_last(former, latter):
    return lax.dot_general(
        former, latter, (((1,), (1,)), ((), ())), preferred_element_type=jnp.float32
    )


def conv_windows(padded, tap_count, length_fine):
    return jnp.concatenate(
        [padded[tap_index : tap_index + length_fine] for tap_index in range(tap_count)], axis=1
    )


def stacked_conv(windows, all_taps):
    tap_count = all_taps.shape[0]
    flat_taps = all_taps.reshape(tap_count * all_taps.shape[1], all_taps.shape[2])
    return jnp.dot(windows, flat_taps, preferred_element_type=jnp.float32)


def on_device(
    binned_signals,
    kernel_coefficients,
    asking_projector,
    lookup_projector,
    content_projector,
    readout_projector,
    logit_multipliers,
    loss_sensitivity,
):
    incoming_tensor = binned_signals[0]
    directional_perturbations = loss_sensitivity[0]
    length_fine = incoming_tensor.shape[0]
    channels = incoming_tensor.shape[1]
    tap_count = kernel_coefficients.shape[0]
    margin = tap_count // 2
    attender_total = logit_multipliers.shape[0]
    probe_extent = asking_projector.shape[1] // attender_total
    value_width = content_projector.shape[1] // attender_total
    raw_padded = padded_2(incoming_tensor, (("seq", 0),), margin)
    padded = activate(layer_norm(raw_padded.astype(jnp.float32))).astype(jnp.bfloat16)
    windows = conv_windows(padded, tap_count, length_fine)
    core = coord("core")
    half_width = kernel_coefficients.shape[2] // 2
    own_half = lax.dynamic_slice_in_dim(kernel_coefficients, core * half_width, half_width, axis=2)
    own_taps = lax.all_gather(own_half, "dp", axis=1, tiled=True)
    other_taps = shift(own_taps, "core", 1)
    conv_own = stacked_conv(windows, own_taps)
    conv_other = stacked_conv(windows, other_taps)
    conv_sum = jnp.where(
        core == 0,
        jnp.concatenate([conv_own, conv_other], axis=1),
        jnp.concatenate([conv_other, conv_own], axis=1),
    )
    summed = incoming_tensor.astype(jnp.float32) + conv_sum
    pooled = jnp.max(summed.reshape(length_fine // POOL, POOL, channels), axis=1).astype(
        jnp.bfloat16
    )
    normed = layer_norm(pooled.astype(jnp.float32)).astype(jnp.bfloat16)
    queries = jnp.dot(normed, asking_projector, preferred_element_type=jnp.float32)
    query_hat, query_factor = head_norm(queries, probe_extent)
    query_unit = query_hat.astype(jnp.bfloat16)
    key_local = head_norm(
        jnp.dot(normed, lookup_projector, preferred_element_type=jnp.float32), probe_extent
    )[0].astype(jnp.bfloat16)
    value_local = jnp.dot(normed, content_projector, preferred_element_type=jnp.float32).astype(
        jnp.bfloat16
    )
    key_width = key_local.shape[1]
    joined = jnp.concatenate([key_local, value_local], axis=1)
    for dim in ("zlo", "y", "core"):
        joined = gather_dim(joined, dim, ordered=False)
    joined = joined.reshape(-1, joined.shape[-1])
    key_unit, values_all = joined[:, :key_width], joined[:, key_width:]
    heads_grad = contract_last(directional_perturbations, readout_projector).astype(jnp.bfloat16)
    outputs = []
    diffs = []
    for attender_slot in range(attender_total):
        key_lo = attender_slot * probe_extent
        value_lo = attender_slot * value_width
        query_part = query_unit[:, key_lo : key_lo + probe_extent]
        key_part = key_unit[:, key_lo : key_lo + probe_extent]
        value_part = values_all[:, value_lo : value_lo + value_width]
        attender_logit_gain = logit_multipliers[attender_slot] / probe_extent
        scores = contract_last(query_part, key_part) * attender_logit_gain
        expo = jnp.exp(scores)
        probs = expo / jnp.sum(expo, axis=1, keepdims=True)
        head_out = jnp.dot(
            probs.astype(jnp.bfloat16), value_part, preferred_element_type=jnp.float32
        )
        outputs.append(head_out)
        grad_part = heads_grad[:, value_lo : value_lo + value_width]
        prob_grad = contract_last(grad_part, value_part)
        delta = jnp.sum(grad_part.astype(jnp.float32) * head_out, axis=1, keepdims=True)
        score_grad = (probs * (prob_grad - delta)).astype(jnp.bfloat16)
        unit_grad = (
            jnp.dot(score_grad, key_part, preferred_element_type=jnp.float32) * attender_logit_gain
        )
        hat_part = query_hat[:, key_lo : key_lo + probe_extent]
        factor_part = query_factor[:, key_lo : key_lo + probe_extent]
        diffs.append(
            factor_part
            * (unit_grad - hat_part * jnp.mean(hat_part * unit_grad, axis=1, keepdims=True))
        )
    heads_low = jnp.concatenate(outputs, axis=1).astype(jnp.bfloat16)
    update = jnp.dot(heads_low, readout_projector, preferred_element_type=jnp.float32)
    query_diff = jnp.concatenate(diffs, axis=1).astype(jnp.bfloat16)
    query_local = contract_first(normed, query_diff)
    out_local = contract_first(heads_low, directional_perturbations)
    flat = all_reduce_flat(jnp.concatenate([query_local.reshape(-1), out_local.reshape(-1)]))
    query_grad = flat[: query_local.size].reshape(query_local.shape)
    out_grad = flat[query_local.size :].reshape(out_local.shape)
    return (pooled[None], update[None], query_grad, out_grad)


def solution(mesh):
    return jax.shard_map(
        on_device,
        mesh=mesh,
        in_specs=(
            P("dp", "seq", None),
            P(None, "dp", None),
            P(),
            P(),
            P(),
            P(),
            P(),
            P("dp", "seq", None),
        ),
        out_specs=(P("dp", "seq", None), P("dp", "seq", None), P(), P()),
        check_vma=False,
    )
```

```python
import jax
import jax.numpy as jnp
from jax import lax
from jax.sharding import PartitionSpec as P

POOL = 4


norm_eps = 1e-05
head_eps = 1e-06


def padded_2(array, sides, width):
    for axis, dim in sides:
        devices, length = (lax.axis_size(axis), array.shape[dim])
        up = [(i, (i + 1) % devices) for i in range(devices - 1)]
        down = [(j, i) for i, j in up]
        last = lax.slice_in_dim(array, length - width, length, axis=dim)
        leading = lax.slice_in_dim(array, 0, width, axis=dim)
        before = lax.ppermute(last, axis, up)
        after = lax.ppermute(leading, axis, down)
        array = jnp.concatenate([before, array, after], axis=dim)
    return array


DIMS = {
    "core": ("seq", 1, 2),
    "zlo": ("seq", 2, 4),
    "y": ("seq", 8, 4),
    "x": ("dp", 1, 4),
    "zhi": ("dp", 4, 4),
}
RS_ORDER = ("core", "y", "x")
SUM_ORDER = ("zlo", "zhi")


def coord(dim):
    axis, stride, size = DIMS[dim]
    return (lax.axis_index(axis) // stride) % size


def shift(array, dim, step):
    axis, stride, size = DIMS[dim]
    pairs = []
    for index in range(lax.axis_size(axis)):
        here = (index // stride) % size
        source = index + ((here + step) % size - here) * stride
        pairs.append((source, index))
    return lax.ppermute(array, axis, pairs)


def reduce_scatter_dim(chunks, dim):
    size = DIMS[dim][2]
    me = coord(dim)
    total = lax.dynamic_index_in_dim(chunks, me, 0, keepdims=False)
    for step in range(1, size):
        part = lax.dynamic_index_in_dim(chunks, (me - step) % size, 0, keepdims=False)
        total = total + shift(part, dim, step)
    return total


def gather_dim(array, dim, ordered=True):
    size = DIMS[dim][2]
    stacked = jnp.stack([array] + [shift(array, dim, step) for step in range(1, size)])
    if ordered and size == 2:
        stacked = jnp.where(coord(dim) == 0, stacked, stacked[::-1])
    elif ordered:
        slots = (jnp.arange(size) - coord(dim)) % size
        stacked = jnp.take(stacked, slots, axis=0, mode="clip")
    return stacked


def sum_in_order(stacked):
    total = stacked[0]
    for index in range(1, stacked.shape[0]):
        total = total + stacked[index]
    return total


def all_reduce_rows(rows):
    sizes = [DIMS[dim][2] for dim in RS_ORDER]
    chunks = rows.reshape(*sizes, -1, rows.shape[1])
    for dim in RS_ORDER:
        chunks = reduce_scatter_dim(chunks, dim)
    for dim in SUM_ORDER:
        chunks = sum_in_order(gather_dim(chunks, dim))
    for dim in reversed(RS_ORDER):
        chunks = gather_dim(chunks, dim)
    return chunks.reshape(rows.shape)


def layer_norm(values):
    centre = jnp.mean(values, axis=-1, keepdims=True)
    shifted = values - centre
    variance = jnp.mean(shifted * shifted, axis=-1, keepdims=True)
    return shifted * lax.rsqrt(variance + norm_eps)


def activate(values):
    return values * jax.nn.sigmoid(1.702 * values)


def head_norm(values, group_width):
    grouped = values.reshape(values.shape[0], -1, group_width)
    factor = lax.rsqrt(jnp.mean(grouped * grouped, axis=-1, keepdims=True) + head_eps)
    return (
        (grouped * factor).reshape(values.shape),
        jnp.broadcast_to(factor, grouped.shape).reshape(values.shape),
    )


def contract_first(former, latter):
    return lax.dot_general(
        former, latter, (((0,), (0,)), ((), ())), preferred_element_type=jnp.float32
    )


def contract_last(former, latter):
    return lax.dot_general(
        former, latter, (((1,), (1,)), ((), ())), preferred_element_type=jnp.float32
    )


def conv_windows(padded, tap_count, length_fine):
    return jnp.concatenate(
        [padded[tap_index : tap_index + length_fine] for tap_index in range(tap_count)], axis=1
    )


def stacked_conv(windows, all_taps):
    tap_count = all_taps.shape[0]
    flat_taps = all_taps.reshape(tap_count * all_taps.shape[1], all_taps.shape[2])
    return jnp.dot(windows, flat_taps, preferred_element_type=jnp.float32)


def on_device(
    binned_signals,
    kernel_coefficients,
    asking_projector,
    lookup_projector,
    content_projector,
    readout_projector,
    logit_multipliers,
    loss_sensitivity,
):
    incoming_tensor = binned_signals[0]
    directional_perturbations = loss_sensitivity[0]
    length_fine = incoming_tensor.shape[0]
    channels = incoming_tensor.shape[1]
    tap_count = kernel_coefficients.shape[0]
    margin = tap_count // 2
    attender_total = logit_multipliers.shape[0]
    probe_extent = asking_projector.shape[1] // attender_total
    value_width = content_projector.shape[1] // attender_total
    raw_padded = padded_2(incoming_tensor, (("seq", 0),), margin)
    padded = activate(layer_norm(raw_padded.astype(jnp.float32))).astype(jnp.bfloat16)
    windows = conv_windows(padded, tap_count, length_fine)
    core = coord("core")
    half_width = kernel_coefficients.shape[2] // 2
    own_half = lax.dynamic_slice_in_dim(kernel_coefficients, core * half_width, half_width, axis=2)
    own_taps = lax.all_gather(own_half, "dp", axis=1, tiled=True)
    other_taps = shift(own_taps, "core", 1)
    conv_own = stacked_conv(windows, own_taps)
    conv_other = stacked_conv(windows, other_taps)
    conv_sum = jnp.where(
        core == 0,
        jnp.concatenate([conv_own, conv_other], axis=1),
        jnp.concatenate([conv_other, conv_own], axis=1),
    )
    summed = incoming_tensor.astype(jnp.float32) + conv_sum
    pooled = jnp.max(summed.reshape(length_fine // POOL, POOL, channels), axis=1).astype(
        jnp.bfloat16
    )
    normed = layer_norm(pooled.astype(jnp.float32)).astype(jnp.bfloat16)
    queries = jnp.dot(normed, asking_projector, preferred_element_type=jnp.float32)
    query_hat, query_factor = head_norm(queries, probe_extent)
    query_unit = query_hat.astype(jnp.bfloat16)
    key_local = head_norm(
        jnp.dot(normed, lookup_projector, preferred_element_type=jnp.float32), probe_extent
    )[0].astype(jnp.bfloat16)
    value_local = jnp.dot(normed, content_projector, preferred_element_type=jnp.float32).astype(
        jnp.bfloat16
    )
    key_width = key_local.shape[1]
    joined = jnp.concatenate([key_local, value_local], axis=1)
    for dim in ("zlo", "y", "core"):
        joined = gather_dim(joined, dim, ordered=False)
    joined = joined.reshape(-1, joined.shape[-1])
    key_unit, values_all = joined[:, :key_width], joined[:, key_width:]
    heads_grad = contract_last(directional_perturbations, readout_projector).astype(jnp.bfloat16)
    outputs = []
    diffs = []
    for attender_slot in range(attender_total):
        key_lo = attender_slot * probe_extent
        value_lo = attender_slot * value_width
        query_part = query_unit[:, key_lo : key_lo + probe_extent]
        key_part = key_unit[:, key_lo : key_lo + probe_extent]
        value_part = values_all[:, value_lo : value_lo + value_width]
        attender_logit_gain = logit_multipliers[attender_slot] / probe_extent
        scores = contract_last(query_part, key_part) * attender_logit_gain
        expo = jnp.exp(scores)
        probs = expo / jnp.sum(expo, axis=1, keepdims=True)
        head_out = jnp.dot(
            probs.astype(jnp.bfloat16), value_part, preferred_element_type=jnp.float32
        )
        outputs.append(head_out)
        grad_part = heads_grad[:, value_lo : value_lo + value_width]
        prob_grad = contract_last(grad_part, value_part)
        delta = jnp.sum(grad_part.astype(jnp.float32) * head_out, axis=1, keepdims=True)
        score_grad = (probs * (prob_grad - delta)).astype(jnp.bfloat16)
        unit_grad = (
            jnp.dot(score_grad, key_part, preferred_element_type=jnp.float32) * attender_logit_gain
        )
        hat_part = query_hat[:, key_lo : key_lo + probe_extent]
        factor_part = query_factor[:, key_lo : key_lo + probe_extent]
        diffs.append(
            factor_part
            * (unit_grad - hat_part * jnp.mean(hat_part * unit_grad, axis=1, keepdims=True))
        )
    heads_low = jnp.concatenate(outputs, axis=1).astype(jnp.bfloat16)
    update = jnp.dot(heads_low, readout_projector, preferred_element_type=jnp.float32)
    query_diff = jnp.concatenate(diffs, axis=1).astype(jnp.bfloat16)
    query_local = contract_first(normed, query_diff)
    out_local = contract_first(heads_low, directional_perturbations)
    width = query_local.shape[1]
    packed = jnp.concatenate([query_local, out_local.reshape(-1, width)], axis=0)
    used_rows = packed.shape[0]
    block = 8
    for dim in RS_ORDER:
        block *= DIMS[dim][2]
    packed = jnp.pad(packed, ((0, -used_rows % block), (0, 0)))
    packed = all_reduce_rows(packed)
    query_grad = packed[: query_local.shape[0]]
    out_grad = packed[query_local.shape[0] : used_rows].reshape(out_local.shape)
    return (pooled[None], update[None], query_grad, out_grad)


def solution(mesh):
    return jax.shard_map(
        on_device,
        mesh=mesh,
        in_specs=(
            P("dp", "seq", None),
            P(None, "dp", None),
            P(),
            P(),
            P(),
            P(),
            P(),
            P("dp", "seq", None),
        ),
        out_specs=(P("dp", "seq", None), P("dp", "seq", None), P(), P()),
        check_vma=False,
    )
```
